32 devices in a mesh: section: 8 (over z, y), tensor: 4 (over x, core).
Axes of the slice: x: 2, y: 2, z: 4, core: 2. Of those that a mesh axis runs over, the one named last changes fastest.
Arguments:
- vision_tokens: bfloat16 [2048, 1664], P('section'), may hold values from -6 to 6
- key_weight: bfloat16 [3328, 8192], P('section', 'tensor'), may hold values from -0.15625 to 0.15625
- value_weight: bfloat16 [3328, 8192], P('section', 'tensor'), may hold values from -0.15625 to 0.15625
- queries: bfloat16 [8, 1024, 8192], P('section', None, 'tensor'), may hold values from -6 to 6
- gate: float32 [2], replicated, may hold values from 0.3 to 1.5
- visible: int32 [4, 4, 4], replicated, may hold values from -1 to 1, as said below
- out_grad: bfloat16 [8, 1024, 8192], P('section', None, 'tensor'), may hold values from -6 to 6
Outputs:
- attended: bfloat16 [8, 1024, 8192], P('section', None, 'tensor')
- vision_grad: bfloat16 [2048, 1664], P('section')
The draws below stay inside these ranges and needn't reach their ends.
Inputs may be any that keep to these rules, and one draw needn't show every extreme that they name: `visible`: each row of 4 entries is non-decreasing, and every image index 0 to 1 occurs in every row.
All inputs are finite; a program needn't handle non-finite values.
Results may differ from the reference program's by a relative error of at most 0.029.
Values may be sent and summed in bfloat16 or wider, within the bound.
No kernel may reach another device: no remote copies, remote signals or barrier semaphores. Data moves between devices by JAX's collectives and lax.ppermute only.
A program may use at most 128 MiB of HBM per device.

```python
import jax
import jax.numpy as jnp
from jax import lax

D = 8192
H = 64
HD = 128
DV = 1664
IMG_TOK = 64
TBLOCK = 64
SEQ = 256
IMGS = 2
SAMPLES = 4
MICRO = 4
TXT = 1024
VTOK = 512
LAYERS = 2


def draw_visible(key, part):
    blocks = SEQ // TBLOCK
    needed = jnp.broadcast_to(jnp.arange(IMGS, dtype=jnp.int32)[None, None, :], (MICRO, SAMPLES, IMGS))
    extra = jax.random.randint(key, (MICRO, SAMPLES, blocks - IMGS), -1, IMGS, dtype=jnp.int32)
    return jnp.sort(jnp.concatenate([needed, extra], axis=2), axis=2).astype(jnp.int32)


def block_scale(rng, extent, cuts, low, largest):
    gain, own = 1.0, jax.random.fold_in(rng, 6)
    for dim, blocks in cuts:
        heights = jnp.exp(jax.random.uniform(jax.random.fold_in(own, dim), (blocks,), jnp.float32, low / len(cuts), largest / len(cuts)))
        gain = gain * jnp.repeat(heights, extent[dim] // blocks).reshape([-1 if axis == dim else 1 for axis in range(len(extent))])
    return gain


def normal_values(key, shape, scale, limit, cuts=(), held_as=jnp.bfloat16):
    entries = scale * jax.random.normal(key, shape, jnp.float32)
    if cuts:
        entries = entries * block_scale(key, shape, cuts, -0.22, 0.18)
    return jnp.clip(entries, -limit, limit).astype(held_as)


def setup_inputs(seed: int = 0) -> dict:
    key_list = jax.random.split(jax.random.key(seed), 8)
    vision_tokens = normal_values(key_list[0], (MICRO * VTOK, DV), 1.0, 6.0, ((0, 8),))
    key_weight = normal_values(key_list[1], (MICRO * LAYERS * (DV // MICRO), D), DV ** -0.5, 0.15625, ((0, 8), (1, 4)))
    value_weight = normal_values(key_list[2], (MICRO * LAYERS * (DV // MICRO), D), DV ** -0.5, 0.15625, ((0, 8), (1, 4)))
    queries = normal_values(key_list[3], (MICRO * LAYERS, TXT, D), 1.0, 6.0, ((0, 8), (2, 4)))
    gate = jnp.clip(jax.random.uniform(key_list[4], (LAYERS,), jnp.float32, 0.3, 1.5), 0.3, 1.5)
    visible = draw_visible(jax.random.fold_in(key_list[7], 71), 0)
    out_grad = normal_values(key_list[6], (MICRO * LAYERS, TXT, D), 1.0, 6.0, ((0, 8), (2, 4)))
    return dict(vision_tokens=vision_tokens, key_weight=key_weight, value_weight=value_weight, queries=queries, gate=gate, visible=visible, out_grad=out_grad)


def block_index(visible):
    samples = visible.shape[0]
    base = jnp.arange(samples, dtype=jnp.int32)[:, None] * IMGS
    seen = (base + jnp.maximum(visible, 0)).reshape(-1).astype(jnp.int32)
    validf = (visible >= 0).reshape(-1).astype(jnp.float32)
    return seen, validf


def local_layer(key_rows, value_rows, query, gate_value, cotangent, visible, heads):
    width = heads * HD
    seen, validf = block_index(visible)
    images = key_rows.shape[0] // IMG_TOK
    key_img = key_rows.reshape(images, IMG_TOK, heads, HD)[seen]
    val_img = value_rows.reshape(images, IMG_TOK, heads, HD)[seen]
    blocks = seen.shape[0]
    query_b = query.reshape(blocks, TBLOCK, heads, HD)
    scale = 1.0 / (HD ** 0.5)
    scores = jnp.einsum("bqhd,bkhd->bhqk", query_b.astype(jnp.float32), key_img.astype(jnp.float32)) * scale
    exponent = jnp.exp(scores)
    probs = exponent / jnp.sum(exponent, axis=-1, keepdims=True) * validf[:, None, None, None]
    probs_b = probs.astype(jnp.bfloat16)
    mixed = jnp.einsum("bhqk,bkhd->bqhd", probs_b.astype(jnp.float32), val_img.astype(jnp.float32))
    factor = jnp.tanh(gate_value)
    attended = (factor * mixed).astype(jnp.bfloat16).reshape(-1, width)
    head_grad = (factor * cotangent.astype(jnp.float32)).astype(jnp.bfloat16).reshape(blocks, TBLOCK, heads, HD)
    vgrad_blk = jnp.einsum("bhqk,bqhd->bkhd", probs_b.astype(jnp.float32), head_grad.astype(jnp.float32))
    prob_grad = jnp.einsum("bqhd,bkhd->bhqk", head_grad.astype(jnp.float32), val_img.astype(jnp.float32))
    delta = jnp.sum(probs * prob_grad, axis=-1, keepdims=True)
    score_grad = (probs * (prob_grad - delta) * scale).astype(jnp.bfloat16)
    kgrad_blk = jnp.einsum("bhqk,bqhd->bkhd", score_grad.astype(jnp.float32), query_b.astype(jnp.float32))
    onehot = (seen[:, None] == jnp.arange(images, dtype=jnp.int32)[None, :]).astype(jnp.float32)
    key_grad = jnp.einsum("bi,bkhd->ikhd", onehot, kgrad_blk).reshape(-1, width).astype(jnp.bfloat16)
    value_grad = jnp.einsum("bi,bkhd->ikhd", onehot, vgrad_blk).reshape(-1, width).astype(jnp.bfloat16)
    return attended, key_grad, value_grad


def reference(vision_tokens, key_weight, value_weight, queries, gate, visible, out_grad):
    w_keys = key_weight.reshape(MICRO, LAYERS, DV // MICRO, D).transpose(1, 0, 2, 3).reshape(LAYERS, DV, D)
    w_values = value_weight.reshape(MICRO, LAYERS, DV // MICRO, D).transpose(1, 0, 2, 3).reshape(LAYERS, DV, D)
    tokens_all = vision_tokens.reshape(MICRO, VTOK, DV)
    query_all = queries.reshape(MICRO, LAYERS, TXT, D)
    grad_all = out_grad.reshape(MICRO, LAYERS, TXT, D)
    outputs = []
    grads = []
    for micro in range(MICRO):
        tokens = tokens_all[micro]
        micro_visible = visible[micro]

        def one_layer(carry, items):
            w_key, w_value, query, gate_value, cotangent = items
            key_rows = jnp.dot(tokens, w_key, preferred_element_type=jnp.float32).astype(jnp.bfloat16)
            value_rows = jnp.dot(tokens, w_value, preferred_element_type=jnp.float32).astype(jnp.bfloat16)
            attended, key_grad, value_grad = local_layer(key_rows, value_rows, query, gate_value, cotangent, micro_visible, H)
            term = lax.dot_general(key_grad, w_key, (((1,), (1,)), ((), ())), preferred_element_type=jnp.float32)
            term = term + lax.dot_general(value_grad, w_value, (((1,), (1,)), ((), ())), preferred_element_type=jnp.float32)
            return carry + term, attended

        start = jnp.zeros(tokens.shape, jnp.float32)
        total, attended = lax.scan(one_layer, start, (w_keys, w_values, query_all[micro], gate, grad_all[micro]))
        outputs.append(attended)
        grads.append(total.astype(jnp.bfloat16))
    attended_all = jnp.concatenate(outputs, axis=0)
    return attended_all, jnp.concatenate(grads, axis=0)
```

```python
import jax
import jax.numpy as jnp
import numpy as np
from jax import lax
from jax.sharding import Mesh
from jax.sharding import PartitionSpec as P

HD = 128
IMG_TOK = 64
TBLOCK = 64
IMGS = 2
MICRO = 4


def block_index(visible):
    samples = visible.shape[0]
    base = jnp.arange(samples, dtype=jnp.int32)[:, None] * IMGS
    seen = (base + jnp.maximum(visible, 0)).reshape(-1)
    validf = (visible >= 0).reshape(-1).astype(jnp.float32)
    return (seen, validf)


def local_layer(key_rows, value_rows, query, gate_value, cotangent, visible, heads):
    width = heads * HD
    seen, validf = block_index(visible)
    images = key_rows.shape[0] // IMG_TOK
    key_img = jnp.take(key_rows.reshape(images, IMG_TOK, heads, HD), seen, axis=0)
    val_img = jnp.take(value_rows.reshape(images, IMG_TOK, heads, HD), seen, axis=0)
    blocks = seen.shape[0]
    query_b = query.reshape(blocks, TBLOCK, heads, HD)
    scale = 1.0 / HD**0.5
    scores = (
        jnp.einsum("bqhd,bkhd->bhqk", query_b, key_img, preferred_element_type=jnp.float32) * scale
    )
    exponent = jnp.exp(scores)
    probs = exponent / jnp.sum(exponent, axis=-1, keepdims=True) * validf[:, None, None, None]
    probs_b = probs.astype(jnp.bfloat16)
    mixed = jnp.einsum("bhqk,bkhd->bqhd", probs_b, val_img, preferred_element_type=jnp.float32)
    factor = jnp.tanh(gate_value)
    attended = (factor * mixed).astype(jnp.bfloat16).reshape(-1, width)
    head_grad = (
        (factor * cotangent.astype(jnp.float32))
        .astype(jnp.bfloat16)
        .reshape(blocks, TBLOCK, heads, HD)
    )
    vgrad_blk = jnp.einsum(
        "bhqk,bqhd->bkhd", probs_b, head_grad, preferred_element_type=jnp.float32
    )
    prob_grad = jnp.einsum(
        "bqhd,bkhd->bhqk", head_grad, val_img, preferred_element_type=jnp.float32
    )
    delta = jnp.sum(probs * prob_grad, axis=-1, keepdims=True)
    score_grad = (probs * (prob_grad - delta) * scale).astype(jnp.bfloat16)
    kgrad_blk = jnp.einsum(
        "bhqk,bqhd->bkhd", score_grad, query_b, preferred_element_type=jnp.float32
    )
    onehot = (seen[:, None] == jnp.arange(images, dtype=jnp.int32)[None, :]).astype(jnp.float32)
    key_grad = (
        jnp.einsum("bi,bkhd->ikhd", onehot, kgrad_blk).reshape(-1, width).astype(jnp.bfloat16)
    )
    value_grad = (
        jnp.einsum("bi,bkhd->ikhd", onehot, vgrad_blk).reshape(-1, width).astype(jnp.bfloat16)
    )
    return (attended, key_grad, value_grad)


def back_product(grad_rows, weight):
    return lax.dot_general(
        grad_rows, weight, (((1,), (1,)), ((), ())), preferred_element_type=jnp.float32
    )


def shards(vision_tokens, key_weight, value_weight, queries, gate, visible, out_grad):
    layer = lax.axis_index("layer")
    micro = lax.axis_index("micro")
    stacked = jnp.stack([key_weight, value_weight])
    stacked = lax.all_gather(stacked, "micro", axis=1, tiled=True)
    w_key = stacked[0]
    w_value = stacked[1]
    width = w_key.shape[1]
    heads = width // HD
    gate_value = lax.dynamic_index_in_dim(gate, layer, 0, keepdims=False)
    own_visible = lax.dynamic_index_in_dim(visible, micro, 0, keepdims=False)
    all_rows = lax.all_gather(vision_tokens, "layer", axis=0, tiled=True)
    key_rows = jnp.dot(all_rows, w_key, preferred_element_type=jnp.float32).astype(jnp.bfloat16)
    value_rows = jnp.dot(all_rows, w_value, preferred_element_type=jnp.float32).astype(jnp.bfloat16)
    attended, key_grad, value_grad = local_layer(
        key_rows, value_rows, queries[0], gate_value, out_grad[0], own_visible, heads
    )
    term = back_product(key_grad, w_key) + back_product(value_grad, w_value)
    part = lax.psum_scatter(term.astype(jnp.bfloat16), "layer", scatter_dimension=0, tiled=True)
    owned = lax.psum(part, "tensor")
    return (attended[None], owned)


def solution(mesh):
    sections, tensors = mesh.devices.shape
    grid = Mesh(
        np.asarray(mesh.devices).reshape(MICRO, sections // MICRO, tensors),
        ("micro", "layer", "tensor"),
    )
    rows = ("micro", "layer")
    placed = (
        P(rows, None),
        P(rows, "tensor"),
        P(rows, "tensor"),
        P(rows, None, "tensor"),
        P(),
        P(),
        P(rows, None, "tensor"),
    )
    return jax.shard_map(
        shards,
        mesh=grid,
        in_specs=placed,
        out_specs=(P(rows, None, "tensor"), P(rows, None)),
        check_vma=False,
    )
```

```python
import jax
import jax.numpy as jnp
import numpy as np
from jax import lax
from jax.sharding import Mesh
from jax.sharding import PartitionSpec as P

HD = 128
IMG_TOK = 64
TBLOCK = 64
IMGS = 2
MICRO = 4
CHUNKS = 4
AHEAD = 4
RELAY = False


def block_index(visible):
    samples = visible.shape[0]
    base = jnp.arange(samples, dtype=jnp.int32)[:, None] * IMGS
    seen = (base + jnp.maximum(visible, 0)).reshape(-1)
    validf = (visible >= 0).reshape(-1).astype(jnp.float32)
    return (seen, validf)


def local_layer(key_rows, value_rows, query, gate_value, cotangent, visible, heads):
    width = heads * HD
    seen, validf = block_index(visible)
    images = key_rows.shape[0] // IMG_TOK
    key_img = jnp.take(key_rows.reshape(images, IMG_TOK, heads, HD), seen, axis=0)
    val_img = jnp.take(value_rows.reshape(images, IMG_TOK, heads, HD), seen, axis=0)
    blocks = seen.shape[0]
    query_b = query.reshape(blocks, TBLOCK, heads, HD)
    scale = 1.0 / HD**0.5
    scores = (
        jnp.einsum("bqhd,bkhd->bhqk", query_b, key_img, preferred_element_type=jnp.float32) * scale
    )
    exponent = jnp.exp(scores)
    probs = exponent / jnp.sum(exponent, axis=-1, keepdims=True) * validf[:, None, None, None]
    probs_b = probs.astype(jnp.bfloat16)
    mixed = jnp.einsum("bhqk,bkhd->bqhd", probs_b, val_img, preferred_element_type=jnp.float32)
    factor = jnp.tanh(gate_value)
    attended = (factor * mixed).astype(jnp.bfloat16).reshape(-1, width)
    head_grad = (
        (factor * cotangent.astype(jnp.float32))
        .astype(jnp.bfloat16)
        .reshape(blocks, TBLOCK, heads, HD)
    )
    vgrad_blk = jnp.einsum(
        "bhqk,bqhd->bkhd", probs_b, head_grad, preferred_element_type=jnp.float32
    )
    prob_grad = jnp.einsum(
        "bqhd,bkhd->bhqk", head_grad, val_img, preferred_element_type=jnp.float32
    )
    delta = jnp.sum(probs * prob_grad, axis=-1, keepdims=True)
    score_grad = (probs * (prob_grad - delta) * scale).astype(jnp.bfloat16)
    kgrad_blk = jnp.einsum(
        "bhqk,bqhd->bkhd", score_grad, query_b, preferred_element_type=jnp.float32
    )
    onehot = (seen[:, None] == jnp.arange(images, dtype=jnp.int32)[None, :]).astype(jnp.float32)
    key_grad = (
        jnp.einsum("bi,bkhd->ikhd", onehot, kgrad_blk).reshape(-1, width).astype(jnp.bfloat16)
    )
    value_grad = (
        jnp.einsum("bi,bkhd->ikhd", onehot, vgrad_blk).reshape(-1, width).astype(jnp.bfloat16)
    )
    return (attended, key_grad, value_grad)


def back_product(grad_rows, weight):
    return lax.dot_general(
        grad_rows, weight, (((1,), (1,)), ((), ())), preferred_element_type=jnp.float32
    )


def shards(vision_tokens, key_weight, value_weight, queries, gate, visible, out_grad):
    layer = lax.axis_index("layer")
    micro = lax.axis_index("micro")
    width = key_weight.shape[1]
    heads = width // HD
    chunks = min(CHUNKS, heads)
    step = width // chunks
    gate_value = lax.dynamic_index_in_dim(gate, layer, 0, keepdims=False)
    own_visible = lax.dynamic_index_in_dim(visible, micro, 0, keepdims=False)
    all_rows = lax.all_gather(vision_tokens, "layer", axis=0, tiled=True)
    term = None
    pieces = []
    gathered = {}

    micros = lax.axis_size("micro")

    def line_gather(own):
        ups, downs = [], []
        up, down = own, own
        for r in range(1, micros):
            up = lax.ppermute(up, "micro", [(i, i + 1) for i in range(r - 1, micros - 1)])
            down = lax.ppermute(down, "micro", [(i + 1, i) for i in range(r - 1, micros - 1)])
            ups.append(up)
            downs.append(down)
        blocks = []
        for q in range(micros):
            which = jnp.where(q == micro, 0, jnp.where(q < micro, micro - q, micros - 1 + q - micro))
            blocks.append(lax.select_n(which, own, *ups, *downs))
        return jnp.concatenate(blocks, axis=1)

    def fetch(j, after):
        cols = slice(j * step, (j + 1) * step)
        stacked = jnp.stack([key_weight[:, cols], value_weight[:, cols]])
        if after is not None:
            stacked, _ = lax.optimization_barrier((stacked, after))
        if RELAY:
            gathered[j] = line_gather(stacked)
        else:
            gathered[j] = lax.all_gather(stacked, "micro", axis=1, tiled=True)

    for j in range(min(AHEAD, chunks)):
        fetch(j, None)
    for j in range(chunks):
        cols = slice(j * step, (j + 1) * step)
        stacked = gathered.pop(j)
        if term is not None:
            stacked, _ = lax.optimization_barrier((stacked, term))
        w_key = stacked[0]
        w_value = stacked[1]
        key_rows = jnp.dot(all_rows, w_key, preferred_element_type=jnp.float32).astype(jnp.bfloat16)
        value_rows = jnp.dot(all_rows, w_value, preferred_element_type=jnp.float32).astype(
            jnp.bfloat16
        )
        attended, key_grad, value_grad = local_layer(
            key_rows,
            value_rows,
            queries[0, :, cols],
            gate_value,
            out_grad[0, :, cols],
            own_visible,
            step // HD,
        )
        pieces.append(attended)
        part = back_product(key_grad, w_key) + back_product(value_grad, w_value)
        term = part if term is None else term + part
        if j + AHEAD < chunks:
            fetch(j + AHEAD, term)
    attended = jnp.concatenate(pieces, axis=1)
    part = lax.psum_scatter(term.astype(jnp.bfloat16), "layer", scatter_dimension=0, tiled=True)
    owned = lax.psum(part, "tensor")
    return (attended[None], owned)


def solution(mesh):
    sections, tensors = mesh.devices.shape
    grid = Mesh(
        np.asarray(mesh.devices).reshape(MICRO, sections // MICRO, tensors),
        ("micro", "layer", "tensor"),
    )
    rows = ("micro", "layer")
    placed = (
        P(rows, None),
        P(rows, "tensor"),
        P(rows, "tensor"),
        P(rows, None, "tensor"),
        P(),
        P(),
        P(rows, None, "tensor"),
    )
    return jax.shard_map(
        shards,
        mesh=grid,
        in_specs=placed,
        out_specs=(P(rows, None, "tensor"), P(rows, None)),
        check_vma=False,
    )
```

```python
import jax
import jax.numpy as jnp
import numpy as np
from jax import lax
from jax.sharding import Mesh
from jax.sharding import PartitionSpec as P

HD = 128
IMG_TOK = 64
TBLOCK = 64
IMGS = 2
MICRO = 4
CHUNKS = 4
AHEAD = 4
RELAY = False


def block_index(visible):
    samples = visible.shape[0]
    base = jnp.arange(samples, dtype=jnp.int32)[:, None] * IMGS
    seen = (base + jnp.maximum(visible, 0)).reshape(-1)
    validf = (visible >= 0).reshape(-1).astype(jnp.float32)
    return (seen, validf)


def local_layer(key_rows, value_rows, query, gate_value, cotangent, visible, heads):
    width = heads * HD
    seen, validf = block_index(visible)
    images = key_rows.shape[0] // IMG_TOK
    key_img = jnp.take(key_rows.reshape(images, IMG_TOK, heads, HD), seen, axis=0)
    val_img = jnp.take(value_rows.reshape(images, IMG_TOK, heads, HD), seen, axis=0)
    blocks = seen.shape[0]
    query_b = query.reshape(blocks, TBLOCK, heads, HD)
    scale = 1.0 / HD**0.5
    scores = (
        jnp.einsum("bqhd,bkhd->bhqk", query_b, key_img, preferred_element_type=jnp.float32) * scale
    )
    exponent = jnp.exp(scores)
    probs = exponent / jnp.sum(exponent, axis=-1, keepdims=True) * validf[:, None, None, None]
    probs_b = probs.astype(jnp.bfloat16)
    mixed = jnp.einsum("bhqk,bkhd->bqhd", probs_b, val_img, preferred_element_type=jnp.float32)
    factor = jnp.tanh(gate_value)
    attended = (factor * mixed).astype(jnp.bfloat16).reshape(-1, width)
    head_grad = (
        (factor * cotangent.astype(jnp.float32))
        .astype(jnp.bfloat16)
        .reshape(blocks, TBLOCK, heads, HD)
    )
    vgrad_blk = jnp.einsum(
        "bhqk,bqhd->bkhd", probs_b, head_grad, preferred_element_type=jnp.float32
    )
    prob_grad = jnp.einsum(
        "bqhd,bkhd->bhqk", head_grad, val_img, preferred_element_type=jnp.float32
    )
    delta = jnp.sum(probs * prob_grad, axis=-1, keepdims=True)
    score_grad = (probs * (prob_grad - delta) * scale).astype(jnp.bfloat16)
    kgrad_blk = jnp.einsum(
        "bhqk,bqhd->bkhd", score_grad, query_b, preferred_element_type=jnp.float32
    )
    onehot = (seen[:, None] == jnp.arange(images, dtype=jnp.int32)[None, :]).astype(jnp.float32)
    key_grad = (
        jnp.einsum("bi,bkhd->ikhd", onehot, kgrad_blk).reshape(-1, width).astype(jnp.bfloat16)
    )
    value_grad = (
        jnp.einsum("bi,bkhd->ikhd", onehot, vgrad_blk).reshape(-1, width).astype(jnp.bfloat16)
    )
    return (attended, key_grad, value_grad)


def back_product(grad_rows, weight):
    return lax.dot_general(
        grad_rows, weight, (((1,), (1,)), ((), ())), preferred_element_type=jnp.float32
    )


def exchange(value, axis, swap):
    return lax.ppermute(value.astype(jnp.bfloat16), axis, swap).astype(jnp.float32)


def chip_reduce(term, layer, swap):
    core = lax.axis_index("core")
    quarter = term.shape[0] // 4
    rows = term.reshape(4, quarter, term.shape[1])
    even = rows[0::2]
    odd = rows[1::2]
    keep = jnp.where(core == 0, even, odd)
    give = jnp.where(core == 0, odd, even)
    halves = keep + exchange(give, "core", swap)
    mine = jnp.where(layer == 0, halves[0], halves[1])
    other = jnp.where(layer == 0, halves[1], halves[0])
    summed = mine + exchange(other, "layer", swap)
    rounded = summed.astype(jnp.bfloat16).astype(jnp.float32)
    total = (rounded + exchange(summed, "tx", swap)).astype(jnp.bfloat16)
    partner = lax.ppermute(total, "core", swap)
    return jnp.where(
        core == 0,
        jnp.concatenate([total, partner], axis=0),
        jnp.concatenate([partner, total], axis=0),
    )


def shards(vision_tokens, key_weight, value_weight, queries, gate, visible, out_grad):
    layer = lax.axis_index("layer")
    micro = lax.axis_index("micro")
    width = key_weight.shape[1]
    heads = width // HD
    chunks = min(CHUNKS, heads)
    step = width // chunks
    gate_value = lax.dynamic_index_in_dim(gate, layer, 0, keepdims=False)
    own_visible = lax.dynamic_index_in_dim(visible, micro, 0, keepdims=False)
    swap = [(0, 1), (1, 0)]
    paired = lax.axis_size("layer") == 2
    if paired:
        partner = lax.ppermute(vision_tokens, "layer", swap)
        all_rows = jnp.where(
            layer == 0,
            jnp.concatenate([vision_tokens, partner], axis=0),
            jnp.concatenate([partner, vision_tokens], axis=0),
        )
    else:
        all_rows = lax.all_gather(vision_tokens, "layer", axis=0, tiled=True)
    term = None
    pieces = []
    gathered = {}

    micros = lax.axis_size("micro")

    def line_gather(own):
        ups, downs = [], []
        up, down = own, own
        for r in range(1, micros):
            up = lax.ppermute(up, "micro", [(i, i + 1) for i in range(r - 1, micros - 1)])
            down = lax.ppermute(down, "micro", [(i + 1, i) for i in range(r - 1, micros - 1)])
            ups.append(up)
            downs.append(down)
        blocks = []
        for q in range(micros):
            which = jnp.where(q == micro, 0, jnp.where(q < micro, micro - q, micros - 1 + q - micro))
            blocks.append(lax.select_n(which, own, *ups, *downs))
        return jnp.concatenate(blocks, axis=1)

    def fetch(j, after):
        cols = slice(j * step, (j + 1) * step)
        stacked = jnp.stack([key_weight[:, cols], value_weight[:, cols]])
        if after is not None:
            stacked, _ = lax.optimization_barrier((stacked, after))
        if RELAY:
            gathered[j] = line_gather(stacked)
        else:
            gathered[j] = lax.all_gather(stacked, "micro", axis=1, tiled=True)

    for j in range(min(AHEAD, chunks)):
        fetch(j, None)
    for j in range(chunks):
        cols = slice(j * step, (j + 1) * step)
        stacked = gathered.pop(j)
        if term is not None:
            stacked, _ = lax.optimization_barrier((stacked, term))
        w_key = stacked[0]
        w_value = stacked[1]
        key_rows = jnp.dot(all_rows, w_key, preferred_element_type=jnp.float32).astype(jnp.bfloat16)
        value_rows = jnp.dot(all_rows, w_value, preferred_element_type=jnp.float32).astype(
            jnp.bfloat16
        )
        attended, key_grad, value_grad = local_layer(
            key_rows,
            value_rows,
            queries[0, :, cols],
            gate_value,
            out_grad[0, :, cols],
            own_visible,
            step // HD,
        )
        pieces.append(attended)
        part = back_product(key_grad, w_key) + back_product(value_grad, w_value)
        term = part if term is None else term + part
        if j + AHEAD < chunks:
            fetch(j + AHEAD, term)
    attended = jnp.concatenate(pieces, axis=1)
    if paired and lax.axis_size("tx") == 2 and lax.axis_size("core") == 2:
        owned = chip_reduce(term, layer, swap)
    else:
        part = lax.psum_scatter(
            term.astype(jnp.bfloat16), "layer", scatter_dimension=0, tiled=True
        )
        owned = lax.psum(part, ("tx", "core"))
    return (attended[None], owned)


def solution(mesh):
    sections, tensors = mesh.devices.shape
    grid = Mesh(
        np.asarray(mesh.devices).reshape(MICRO, sections // MICRO, tensors // 2, 2),
        ("micro", "layer", "tx", "core"),
    )
    rows = ("micro", "layer")
    cols = ("tx", "core")
    placed = (
        P(rows, None),
        P(rows, cols),
        P(rows, cols),
        P(rows, None, cols),
        P(),
        P(),
        P(rows, None, cols),
    )
    return jax.shard_map(
        shards,
        mesh=grid,
        in_specs=placed,
        out_specs=(P(rows, None, cols), P(rows, None)),
        check_vma=False,
    )
```

```python
import jax
import jax.numpy as jnp
import numpy as np
from jax import lax
from jax.experimental import pallas as pl
from jax.experimental.pallas import tpu as pltpu
from jax.sharding import Mesh
from jax.sharding import PartitionSpec as P

HD = 128
IMG_TOK = 64
TBLOCK = 64
IMGS = 2
MICRO = 4
CHUNKS = 4
PARTS = (3, 2, 2, 1)
AHEAD = 8
RELAY = False


def attend_kernel(vis_ref, fac_ref, q_ref, k_ref, v_ref, g_ref, att_ref, kg_ref, vg_ref):
    sample = pl.program_id(0)
    seq = q_ref.shape[0]
    keys = k_ref.shape[0]
    scale = 1.0 / HD**0.5
    factor = fac_ref[0:1, 0:1]
    q = q_ref[...]
    k = k_ref[...]
    v = v_ref[...]
    rows = lax.broadcasted_iota(jnp.int32, (seq, keys), 0) // TBLOCK
    image = lax.broadcasted_iota(jnp.int32, (seq, keys), 1) // IMG_TOK
    sees = jnp.full((seq, keys), -1, jnp.int32)
    for b in range(seq // TBLOCK):
        sees = jnp.where(rows == b, vis_ref[sample, b], sees)
    allowed = image == sees
    valid = sees >= 0
    scores = lax.dot_general(q, k, (((1,), (1,)), ((), ())), preferred_element_type=jnp.float32) * scale
    exponent = jnp.where(allowed, jnp.exp(scores), 0.0)
    total = jnp.sum(exponent, axis=-1, keepdims=True)
    probs = jnp.where(valid, exponent / jnp.where(valid, total, 1.0), 0.0)
    probs_b = probs.astype(jnp.bfloat16)
    mixed = jnp.dot(probs_b, v, preferred_element_type=jnp.float32)
    att_ref[...] = (factor * mixed).astype(att_ref.dtype)
    head_grad = (factor * g_ref[...].astype(jnp.float32)).astype(jnp.bfloat16)
    vg_ref[...] = lax.dot_general(
        probs_b, head_grad, (((0,), (0,)), ((), ())), preferred_element_type=jnp.float32
    ).astype(vg_ref.dtype)
    prob_grad = lax.dot_general(
        head_grad, v, (((1,), (1,)), ((), ())), preferred_element_type=jnp.float32
    )
    delta = jnp.sum(probs * prob_grad, axis=-1, keepdims=True)
    score_grad = (probs * (prob_grad - delta) * scale).astype(jnp.bfloat16)
    kg_ref[...] = lax.dot_general(
        score_grad, q, (((0,), (0,)), ((), ())), preferred_element_type=jnp.float32
    ).astype(kg_ref.dtype)


def attend(key_rows, value_rows, query, cotangent, factor, visible, first_head, heads):
    samples = visible.shape[0]
    seq = query.shape[1] // samples
    keys = key_rows.shape[0] // samples
    fac = jnp.full((8, 128), factor, jnp.float32)
    text_spec = pl.BlockSpec((None, seq, HD), lambda s, h, vis: (0, s, first_head + h))
    image_spec = pl.BlockSpec((keys, HD), lambda s, h, vis: (s, h))
    return pl.pallas_call(
        attend_kernel,
        grid_spec=pltpu.PrefetchScalarGridSpec(
            num_scalar_prefetch=1,
            grid=(samples, heads),
            in_specs=[
                pl.BlockSpec((8, 128), lambda s, h, vis: (0, 0)),
                text_spec,
                image_spec,
                image_spec,
                text_spec,
            ],
            out_specs=[
                pl.BlockSpec((seq, HD), lambda s, h, vis: (s, h)),
                image_spec,
                image_spec,
            ],
        ),
        out_shape=[
            jax.ShapeDtypeStruct((query.shape[1], heads * HD), jnp.bfloat16),
            jax.ShapeDtypeStruct(key_rows.shape, jnp.bfloat16),
            jax.ShapeDtypeStruct(key_rows.shape, jnp.bfloat16),
        ],
    )(visible, fac, query, key_rows, value_rows, cotangent)


def back_product(grad_rows, weight):
    return lax.dot_general(
        grad_rows, weight, (((1,), (1,)), ((), ())), preferred_element_type=jnp.float32
    )


def exchange(value, axis, swap):
    return lax.ppermute(value.astype(jnp.bfloat16), axis, swap).astype(jnp.float32)


def chip_reduce(term, layer, swap):
    core = lax.axis_index("core")
    quarter = term.shape[0] // 4
    rows = term.reshape(4, quarter, term.shape[1])
    even = rows[0::2]
    odd = rows[1::2]
    keep = jnp.where(core == 0, even, odd)
    give = jnp.where(core == 0, odd, even)
    halves = keep + exchange(give, "core", swap)
    mine = jnp.where(layer == 0, halves[0], halves[1])
    other = jnp.where(layer == 0, halves[1], halves[0])
    summed = mine + exchange(other, "layer", swap)
    rounded = summed.astype(jnp.bfloat16).astype(jnp.float32)
    total = (rounded + exchange(summed, "tx", swap)).astype(jnp.bfloat16)
    partner = lax.ppermute(total, "core", swap)
    return jnp.where(
        core == 0,
        jnp.concatenate([total, partner], axis=0),
        jnp.concatenate([partner, total], axis=0),
    )


def shards(vision_tokens, key_weight, value_weight, queries, gate, visible, out_grad):
    layer = lax.axis_index("layer")
    micro = lax.axis_index("micro")
    width = key_weight.shape[1]
    heads = width // HD
    if heads % sum(PARTS) == 0:
        unit = heads // sum(PARTS)
        sizes = [part * unit * HD for part in PARTS]
    else:
        chunks = min(CHUNKS, heads)
        sizes = [width // chunks] * chunks
    chunks = len(sizes)
    starts = [sum(sizes[:j]) for j in range(chunks)]
    gate_value = lax.dynamic_index_in_dim(gate, layer, 0, keepdims=False)
    factor = jnp.tanh(gate_value)
    own_visible = lax.dynamic_index_in_dim(visible, micro, 0, keepdims=False)
    swap = [(0, 1), (1, 0)]
    paired = lax.axis_size("layer") == 2
    if paired:
        partner = lax.ppermute(vision_tokens, "layer", swap)
        all_rows = jnp.where(
            layer == 0,
            jnp.concatenate([vision_tokens, partner], axis=0),
            jnp.concatenate([partner, vision_tokens], axis=0),
        )
    else:
        all_rows = lax.all_gather(vision_tokens, "layer", axis=0, tiled=True)
    term = None
    pieces = []
    gathered = {}

    micros = lax.axis_size("micro")

    def line_gather(own):
        ups, downs = [], []
        up, down = own, own
        for r in range(1, micros):
            up = lax.ppermute(up, "micro", [(i, i + 1) for i in range(r - 1, micros - 1)])
            down = lax.ppermute(down, "micro", [(i + 1, i) for i in range(r - 1, micros - 1)])
            ups.append(up)
            downs.append(down)
        blocks = []
        for q in range(micros):
            which = jnp.where(q == micro, 0, jnp.where(q < micro, micro - q, micros - 1 + q - micro))
            blocks.append(lax.select_n(which, own, *ups, *downs))
        return jnp.concatenate(blocks, axis=1)

    def fetch(j, after):
        cols = slice(starts[j], starts[j] + sizes[j])
        stacked = jnp.stack([key_weight[:, cols], value_weight[:, cols]])
        if after is not None:
            stacked, _ = lax.optimization_barrier((stacked, after))
        if RELAY:
            gathered[j] = line_gather(stacked)
        else:
            gathered[j] = lax.all_gather(stacked, "micro", axis=1, tiled=True)

    for j in range(min(AHEAD, chunks)):
        fetch(j, None)
    for j in range(chunks):
        cols = slice(starts[j], starts[j] + sizes[j])
        stacked = gathered.pop(j)
        if term is not None:
            stacked, _ = lax.optimization_barrier((stacked, term))
        w_key = stacked[0]
        w_value = stacked[1]
        key_rows = jnp.dot(all_rows, w_key, preferred_element_type=jnp.float32).astype(jnp.bfloat16)
        value_rows = jnp.dot(all_rows, w_value, preferred_element_type=jnp.float32).astype(
            jnp.bfloat16
        )
        attended, key_grad, value_grad = attend(
            key_rows,
            value_rows,
            queries,
            out_grad,
            factor,
            own_visible,
            starts[j] // HD,
            sizes[j] // HD,
        )
        pieces.append(attended)
        part = back_product(key_grad, w_key) + back_product(value_grad, w_value)
        term = part if term is None else term + part
        if j + AHEAD < chunks:
            fetch(j + AHEAD, term)
    attended = jnp.concatenate(pieces, axis=1)
    if paired and lax.axis_size("tx") == 2 and lax.axis_size("core") == 2:
        owned = chip_reduce(term, layer, swap)
    else:
        part = lax.psum_scatter(
            term.astype(jnp.bfloat16), "layer", scatter_dimension=0, tiled=True
        )
        owned = lax.psum(part, ("tx", "core"))
    return (attended[None], owned)


def solution(mesh):
    sections, tensors = mesh.devices.shape
    grid = Mesh(
        np.asarray(mesh.devices).reshape(MICRO, sections // MICRO, tensors // 2, 2),
        ("micro", "layer", "tx", "core"),
    )
    rows = ("micro", "layer")
    cols = ("tx", "core")
    placed = (
        P(rows, None),
        P(rows, cols),
        P(rows, cols),
        P(rows, None, cols),
        P(),
        P(),
        P(rows, None, cols),
    )
    return jax.shard_map(
        shards,
        mesh=grid,
        in_specs=placed,
        out_specs=(P(rows, None, cols), P(rows, None)),
        check_vma=False,
    )
```

```python
import jax
import jax.numpy as jnp
import numpy as np
from jax import lax
from jax.experimental import pallas as pl
from jax.experimental.pallas import tpu as pltpu
from jax.sharding import Mesh
from jax.sharding import PartitionSpec as P

HD = 128
IMG_TOK = 64
TBLOCK = 64
IMGS = 2
MICRO = 4
CHUNKS = 4
PARTS = (3, 1)
AHEAD = 8
RELAY = False


def attend_kernel(vis_ref, fac_ref, q_ref, k_ref, v_ref, g_ref, att_ref, kg_ref, vg_ref):
    sample = pl.program_id(0)
    seq = q_ref.shape[0]
    keys = k_ref.shape[0]
    scale = 1.0 / HD**0.5
    factor = fac_ref[0:1, 0:1]
    q = q_ref[...]
    k = k_ref[...]
    v = v_ref[...]
    rows = lax.broadcasted_iota(jnp.int32, (seq, keys), 0) // TBLOCK
    image = lax.broadcasted_iota(jnp.int32, (seq, keys), 1) // IMG_TOK
    sees = jnp.full((seq, keys), -1, jnp.int32)
    for b in range(seq // TBLOCK):
        sees = jnp.where(rows == b, vis_ref[sample, b], sees)
    allowed = image == sees
    valid = sees >= 0
    scores = lax.dot_general(q, k, (((1,), (1,)), ((), ())), preferred_element_type=jnp.float32) * scale
    exponent = jnp.where(allowed, jnp.exp(scores), 0.0)
    total = jnp.sum(exponent, axis=-1, keepdims=True)
    probs = jnp.where(valid, exponent / jnp.where(valid, total, 1.0), 0.0)
    probs_b = probs.astype(jnp.bfloat16)
    mixed = jnp.dot(probs_b, v, preferred_element_type=jnp.float32)
    att_ref[...] = (factor * mixed).astype(att_ref.dtype)
    head_grad = (factor * g_ref[...].astype(jnp.float32)).astype(jnp.bfloat16)
    vg_ref[...] = lax.dot_general(
        probs_b, head_grad, (((0,), (0,)), ((), ())), preferred_element_type=jnp.float32
    ).astype(vg_ref.dtype)
    prob_grad = lax.dot_general(
        head_grad, v, (((1,), (1,)), ((), ())), preferred_element_type=jnp.float32
    )
    delta = jnp.sum(probs * prob_grad, axis=-1, keepdims=True)
    score_grad = (probs * (prob_grad - delta) * scale).astype(jnp.bfloat16)
    kg_ref[...] = lax.dot_general(
        score_grad, q, (((0,), (0,)), ((), ())), preferred_element_type=jnp.float32
    ).astype(kg_ref.dtype)


def attend(key_rows, value_rows, query, cotangent, factor, visible, first_head, heads):
    samples = visible.shape[0]
    seq = query.shape[1] // samples
    keys = key_rows.shape[0] // samples
    fac = jnp.full((8, 128), factor, jnp.float32)
    text_spec = pl.BlockSpec((None, seq, HD), lambda s, h, vis: (0, s, first_head + h))
    image_spec = pl.BlockSpec((keys, HD), lambda s, h, vis: (s, h))
    return pl.pallas_call(
        attend_kernel,
        grid_spec=pltpu.PrefetchScalarGridSpec(
            num_scalar_prefetch=1,
            grid=(samples, heads),
            in_specs=[
                pl.BlockSpec((8, 128), lambda s, h, vis: (0, 0)),
                text_spec,
                image_spec,
                image_spec,
                text_spec,
            ],
            out_specs=[
                pl.BlockSpec((seq, HD), lambda s, h, vis: (s, h)),
                image_spec,
                image_spec,
            ],
        ),
        out_shape=[
            jax.ShapeDtypeStruct((query.shape[1], heads * HD), jnp.bfloat16),
            jax.ShapeDtypeStruct(key_rows.shape, jnp.bfloat16),
            jax.ShapeDtypeStruct(key_rows.shape, jnp.bfloat16),
        ],
    )(visible, fac, query, key_rows, value_rows, cotangent)


def back_product(grad_rows, weight):
    return lax.dot_general(
        grad_rows, weight, (((1,), (1,)), ((), ())), preferred_element_type=jnp.float32
    )


def exchange(value, axis, swap):
    return lax.ppermute(value.astype(jnp.bfloat16), axis, swap).astype(jnp.float32)


def chip_reduce(term, layer, swap):
    core = lax.axis_index("core")
    quarter = term.shape[0] // 4
    rows = term.reshape(4, quarter, term.shape[1])
    even = rows[0::2]
    odd = rows[1::2]
    keep = jnp.where(core == 0, even, odd)
    give = jnp.where(core == 0, odd, even)
    halves = keep + exchange(give, "core", swap)
    mine = jnp.where(layer == 0, halves[0], halves[1])
    other = jnp.where(layer == 0, halves[1], halves[0])
    summed = mine + exchange(other, "layer", swap)
    rounded = summed.astype(jnp.bfloat16).astype(jnp.float32)
    total = (rounded + exchange(summed, "tx", swap)).astype(jnp.bfloat16)
    partner = lax.ppermute(total, "core", swap)
    return jnp.where(
        core == 0,
        jnp.concatenate([total, partner], axis=0),
        jnp.concatenate([partner, total], axis=0),
    )


def shards(vision_tokens, key_weight, value_weight, queries, gate, visible, out_grad):
    layer = lax.axis_index("layer")
    micro = lax.axis_index("micro")
    width = key_weight.shape[1]
    heads = width // HD
    if heads % sum(PARTS) == 0:
        unit = heads // sum(PARTS)
        sizes = [part * unit * HD for part in PARTS]
    else:
        chunks = min(CHUNKS, heads)
        sizes = [width // chunks] * chunks
    chunks = len(sizes)
    starts = [sum(sizes[:j]) for j in range(chunks)]
    gate_value = lax.dynamic_index_in_dim(gate, layer, 0, keepdims=False)
    factor = jnp.tanh(gate_value)
    own_visible = lax.dynamic_index_in_dim(visible, micro, 0, keepdims=False)
    swap = [(0, 1), (1, 0)]
    paired = lax.axis_size("layer") == 2
    if paired:
        partner = lax.ppermute(vision_tokens, "layer", swap)
        all_rows = jnp.where(
            layer == 0,
            jnp.concatenate([vision_tokens, partner], axis=0),
            jnp.concatenate([partner, vision_tokens], axis=0),
        )
    else:
        all_rows = lax.all_gather(vision_tokens, "layer", axis=0, tiled=True)
    term = None
    pieces = []
    gathered = {}

    micros = lax.axis_size("micro")

    def line_gather(own):
        ups, downs = [], []
        up, down = own, own
        for r in range(1, micros):
            up = lax.ppermute(up, "micro", [(i, i + 1) for i in range(r - 1, micros - 1)])
            down = lax.ppermute(down, "micro", [(i + 1, i) for i in range(r - 1, micros - 1)])
            ups.append(up)
            downs.append(down)
        blocks = []
        for q in range(micros):
            which = jnp.where(q == micro, 0, jnp.where(q < micro, micro - q, micros - 1 + q - micro))
            blocks.append(lax.select_n(which, own, *ups, *downs))
        return jnp.concatenate(blocks, axis=1)

    def fetch(j, after):
        cols = slice(starts[j], starts[j] + sizes[j])
        stacked = jnp.stack([key_weight[:, cols], value_weight[:, cols]])
        if after is not None:
            stacked, _ = lax.optimization_barrier((stacked, after))
        if RELAY:
            gathered[j] = line_gather(stacked)
        else:
            gathered[j] = lax.all_gather(stacked, "micro", axis=1, tiled=True)

    for j in range(min(AHEAD, chunks)):
        fetch(j, None)
    for j in range(chunks):
        cols = slice(starts[j], starts[j] + sizes[j])
        stacked = gathered.pop(j)
        if term is not None:
            stacked, _ = lax.optimization_barrier((stacked, term))
        w_key = stacked[0]
        w_value = stacked[1]
        key_rows = jnp.dot(all_rows, w_key, preferred_element_type=jnp.float32).astype(jnp.bfloat16)
        value_rows = jnp.dot(all_rows, w_value, preferred_element_type=jnp.float32).astype(
            jnp.bfloat16
        )
        attended, key_grad, value_grad = attend(
            key_rows,
            value_rows,
            queries,
            out_grad,
            factor,
            own_visible,
            starts[j] // HD,
            sizes[j] // HD,
        )
        pieces.append(attended)
        part = back_product(key_grad, w_key) + back_product(value_grad, w_value)
        term = part if term is None else term + part
        if j + AHEAD < chunks:
            fetch(j + AHEAD, term)
    attended = jnp.concatenate(pieces, axis=1)
    if paired and lax.axis_size("tx") == 2 and lax.axis_size("core") == 2:
        owned = chip_reduce(term, layer, swap)
    else:
        part = lax.psum_scatter(
            term.astype(jnp.bfloat16), "layer", scatter_dimension=0, tiled=True
        )
        owned = lax.psum(part, ("tx", "core"))
    return (attended[None], owned)


def solution(mesh):
    sections, tensors = mesh.devices.shape
    grid = Mesh(
        np.asarray(mesh.devices).reshape(MICRO, sections // MICRO, tensors // 2, 2),
        ("micro", "layer", "tx", "core"),
    )
    rows = ("micro", "layer")
    cols = ("tx", "core")
    placed = (
        P(rows, None),
        P(rows, cols),
        P(rows, cols),
        P(rows, None, cols),
        P(),
        P(),
        P(rows, None, cols),
    )
    return jax.shard_map(
        shards,
        mesh=grid,
        in_specs=placed,
        out_specs=(P(rows, None, cols), P(rows, None)),
        check_vma=False,
    )
```

```python
import jax
import jax.numpy as jnp
import numpy as np
from jax import lax
from jax.experimental import pallas as pl
from jax.experimental.pallas import tpu as pltpu
from jax.sharding import Mesh
from jax.sharding import PartitionSpec as P

HD = 128
IMG_TOK = 64
TBLOCK = 64
IMGS = 2
MICRO = 4
CHUNKS = 4
PARTS = (3, 1)
AHEAD = 8
RELAY = False


def attend_kernel(vis_ref, fac_ref, q_ref, k_ref, v_ref, g_ref, att_ref, kg_ref, vg_ref):
    sample = pl.program_id(0)
    seq = q_ref.shape[0]
    keys = k_ref.shape[0]
    scale = 1.0 / HD**0.5
    factor = fac_ref[0:1, 0:1]
    rows = lax.broadcasted_iota(jnp.int32, (seq, keys), 0) // TBLOCK
    image = lax.broadcasted_iota(jnp.int32, (seq, keys), 1) // IMG_TOK
    sees = jnp.full((seq, keys), -1, jnp.int32)
    for b in range(seq // TBLOCK):
        sees = jnp.where(rows == b, vis_ref[sample, b], sees)
    allowed = image == sees
    valid = sees >= 0
    for h in range(q_ref.shape[1] // HD):
        cols = pl.ds(h * HD, HD)
        q = q_ref[:, cols]
        k = k_ref[:, cols]
        v = v_ref[:, cols]
        scores = (
            lax.dot_general(q, k, (((1,), (1,)), ((), ())), preferred_element_type=jnp.float32)
            * scale
        )
        exponent = jnp.where(allowed, jnp.exp(scores), 0.0)
        total = jnp.sum(exponent, axis=-1, keepdims=True)
        probs = jnp.where(valid, exponent / jnp.where(valid, total, 1.0), 0.0)
        probs_b = probs.astype(jnp.bfloat16)
        mixed = jnp.dot(probs_b, v, preferred_element_type=jnp.float32)
        att_ref[:, cols] = (factor * mixed).astype(att_ref.dtype)
        head_grad = (factor * g_ref[:, cols].astype(jnp.float32)).astype(jnp.bfloat16)
        vg_ref[:, cols] = lax.dot_general(
            probs_b, head_grad, (((0,), (0,)), ((), ())), preferred_element_type=jnp.float32
        ).astype(vg_ref.dtype)
        prob_grad = lax.dot_general(
            head_grad, v, (((1,), (1,)), ((), ())), preferred_element_type=jnp.float32
        )
        delta = jnp.sum(probs * prob_grad, axis=-1, keepdims=True)
        score_grad = (probs * (prob_grad - delta) * scale).astype(jnp.bfloat16)
        kg_ref[:, cols] = lax.dot_general(
            score_grad, q, (((0,), (0,)), ((), ())), preferred_element_type=jnp.float32
        ).astype(kg_ref.dtype)


def attend(key_rows, value_rows, query, cotangent, factor, visible, first_head, heads):
    samples = visible.shape[0]
    seq = query.shape[1] // samples
    keys = key_rows.shape[0] // samples
    fac = jnp.full((8, 128), factor, jnp.float32)
    group = heads if first_head % heads == 0 else 1
    wide = group * HD
    text_spec = pl.BlockSpec(
        (None, seq, wide), lambda s, h, vis: (0, s, first_head // group + h)
    )
    image_spec = pl.BlockSpec((keys, wide), lambda s, h, vis: (s, h))
    return pl.pallas_call(
        attend_kernel,
        grid_spec=pltpu.PrefetchScalarGridSpec(
            num_scalar_prefetch=1,
            grid=(samples, heads // group),
            in_specs=[
                pl.BlockSpec((8, 128), lambda s, h, vis: (0, 0)),
                text_spec,
                image_spec,
                image_spec,
                text_spec,
            ],
            out_specs=[
                pl.BlockSpec((seq, wide), lambda s, h, vis: (s, h)),
                image_spec,
                image_spec,
            ],
        ),
        out_shape=[
            jax.ShapeDtypeStruct((query.shape[1], heads * HD), jnp.bfloat16),
            jax.ShapeDtypeStruct(key_rows.shape, jnp.bfloat16),
            jax.ShapeDtypeStruct(key_rows.shape, jnp.bfloat16),
        ],
    )(visible, fac, query, key_rows, value_rows, cotangent)


def back_product(grad_rows, weight):
    return lax.dot_general(
        grad_rows, weight, (((1,), (1,)), ((), ())), preferred_element_type=jnp.float32
    )


def exchange(value, axis, swap):
    return lax.ppermute(value.astype(jnp.bfloat16), axis, swap).astype(jnp.float32)


def chip_reduce(term, layer, swap):
    core = lax.axis_index("core")
    quarter = term.shape[0] // 4
    rows = term.reshape(4, quarter, term.shape[1])
    even = rows[0::2]
    odd = rows[1::2]
    keep = jnp.where(core == 0, even, odd)
    give = jnp.where(core == 0, odd, even)
    halves = keep + exchange(give, "core", swap)
    mine = jnp.where(layer == 0, halves[0], halves[1])
    other = jnp.where(layer == 0, halves[1], halves[0])
    summed = mine + exchange(other, "layer", swap)
    rounded = summed.astype(jnp.bfloat16).astype(jnp.float32)
    total = (rounded + exchange(summed, "tx", swap)).astype(jnp.bfloat16)
    partner = lax.ppermute(total, "core", swap)
    return jnp.where(
        core == 0,
        jnp.concatenate([total, partner], axis=0),
        jnp.concatenate([partner, total], axis=0),
    )


def shards(vision_tokens, key_weight, value_weight, queries, gate, visible, out_grad):
    layer = lax.axis_index("layer")
    micro = lax.axis_index("micro")
    width = key_weight.shape[1]
    heads = width // HD
    if heads % sum(PARTS) == 0:
        unit = heads // sum(PARTS)
        sizes = [part * unit * HD for part in PARTS]
    else:
        chunks = min(CHUNKS, heads)
        sizes = [width // chunks] * chunks
    chunks = len(sizes)
    starts = [sum(sizes[:j]) for j in range(chunks)]
    gate_value = lax.dynamic_index_in_dim(gate, layer, 0, keepdims=False)
    factor = jnp.tanh(gate_value)
    own_visible = lax.dynamic_index_in_dim(visible, micro, 0, keepdims=False)
    swap = [(0, 1), (1, 0)]
    paired = lax.axis_size("layer") == 2
    if paired:
        partner = lax.ppermute(vision_tokens, "layer", swap)
        all_rows = jnp.where(
            layer == 0,
            jnp.concatenate([vision_tokens, partner], axis=0),
            jnp.concatenate([partner, vision_tokens], axis=0),
        )
    else:
        all_rows = lax.all_gather(vision_tokens, "layer", axis=0, tiled=True)
    term = None
    pieces = []
    gathered = {}

    micros = lax.axis_size("micro")

    def line_gather(own):
        ups, downs = [], []
        up, down = own, own
        for r in range(1, micros):
            up = lax.ppermute(up, "micro", [(i, i + 1) for i in range(r - 1, micros - 1)])
            down = lax.ppermute(down, "micro", [(i + 1, i) for i in range(r - 1, micros - 1)])
            ups.append(up)
            downs.append(down)
        blocks = []
        for q in range(micros):
            which = jnp.where(q == micro, 0, jnp.where(q < micro, micro - q, micros - 1 + q - micro))
            blocks.append(lax.select_n(which, own, *ups, *downs))
        return jnp.concatenate(blocks, axis=1)

    def fetch(j, after):
        cols = slice(starts[j], starts[j] + sizes[j])
        stacked = jnp.stack([key_weight[:, cols], value_weight[:, cols]])
        if after is not None:
            stacked, _ = lax.optimization_barrier((stacked, after))
        if RELAY:
            gathered[j] = line_gather(stacked)
        else:
            gathered[j] = lax.all_gather(stacked, "micro", axis=1, tiled=True)

    for j in range(min(AHEAD, chunks)):
        fetch(j, None)
    for j in range(chunks):
        cols = slice(starts[j], starts[j] + sizes[j])
        stacked = gathered.pop(j)
        if term is not None:
            stacked, _ = lax.optimization_barrier((stacked, term))
        w_key = stacked[0]
        w_value = stacked[1]
        key_rows = jnp.dot(all_rows, w_key, preferred_element_type=jnp.float32).astype(jnp.bfloat16)
        value_rows = jnp.dot(all_rows, w_value, preferred_element_type=jnp.float32).astype(
            jnp.bfloat16
        )
        attended, key_grad, value_grad = attend(
            key_rows,
            value_rows,
            queries,
            out_grad,
            factor,
            own_visible,
            starts[j] // HD,
            sizes[j] // HD,
        )
        pieces.append(attended)
        part = back_product(key_grad, w_key) + back_product(value_grad, w_value)
        term = part if term is None else term + part
        if j + AHEAD < chunks:
            fetch(j + AHEAD, term)
    attended = jnp.concatenate(pieces, axis=1)
    if paired and lax.axis_size("tx") == 2 and lax.axis_size("core") == 2:
        owned = chip_reduce(term, layer, swap)
    else:
        part = lax.psum_scatter(
            term.astype(jnp.bfloat16), "layer", scatter_dimension=0, tiled=True
        )
        owned = lax.psum(part, ("tx", "core"))
    return (attended[None], owned)


def solution(mesh):
    sections, tensors = mesh.devices.shape
    grid = Mesh(
        np.asarray(mesh.devices).reshape(MICRO, sections // MICRO, tensors // 2, 2),
        ("micro", "layer", "tx", "core"),
    )
    rows = ("micro", "layer")
    cols = ("tx", "core")
    placed = (
        P(rows, None),
        P(rows, cols),
        P(rows, cols),
        P(rows, None, cols),
        P(),
        P(),
        P(rows, None, cols),
    )
    return jax.shard_map(
        shards,
        mesh=grid,
        in_specs=placed,
        out_specs=(P(rows, None, cols), P(rows, None)),
        check_vma=False,
    )
```

```python
import jax
import jax.numpy as jnp
import numpy as np
from jax import lax
from jax.experimental import pallas as pl
from jax.experimental.pallas import tpu as pltpu
from jax.sharding import Mesh
from jax.sharding import PartitionSpec as P

HD = 128
IMG_TOK = 64
TBLOCK = 64
IMGS = 2
MICRO = 4
CHUNKS = 4
PARTS = (3, 1)
AHEAD = 8
RELAY = False


def attend_kernel(vis_ref, fac_ref, q_ref, k_ref, v_ref, g_ref, att_ref, kg_ref, vg_ref):
    sample = pl.program_id(0)
    seq = q_ref.shape[0]
    keys = k_ref.shape[0]
    scale = 1.0 / HD**0.5
    factor = fac_ref[0:1, 0:1]
    rows = lax.broadcasted_iota(jnp.int32, (seq, keys), 0) // TBLOCK
    image = lax.broadcasted_iota(jnp.int32, (seq, keys), 1) // IMG_TOK
    sees = jnp.full((seq, keys), -1, jnp.int32)
    for b in range(seq // TBLOCK):
        sees = jnp.where(rows == b, vis_ref[sample, b], sees)
    allowed = image == sees
    valid = sees >= 0
    for h in range(q_ref.shape[1] // HD):
        cols = pl.ds(h * HD, HD)
        q = q_ref[:, cols]
        k = k_ref[:, cols]
        v = v_ref[:, cols]
        scores = (
            lax.dot_general(q, k, (((1,), (1,)), ((), ())), preferred_element_type=jnp.float32)
            * scale
        )
        exponent = jnp.where(allowed, jnp.exp(scores), 0.0)
        total = jnp.sum(exponent, axis=-1, keepdims=True)
        probs = jnp.where(valid, exponent / jnp.where(valid, total, 1.0), 0.0)
        probs_b = probs.astype(jnp.bfloat16)
        mixed = jnp.dot(probs_b, v, preferred_element_type=jnp.float32)
        att_ref[:, cols] = (factor * mixed).astype(att_ref.dtype)
        head_grad = (factor * g_ref[:, cols].astype(jnp.float32)).astype(jnp.bfloat16)
        vg_ref[:, cols] = lax.dot_general(
            probs_b, head_grad, (((0,), (0,)), ((), ())), preferred_element_type=jnp.float32
        ).astype(vg_ref.dtype)
        prob_grad = lax.dot_general(
            head_grad, v, (((1,), (1,)), ((), ())), preferred_element_type=jnp.float32
        )
        delta = jnp.sum(probs * prob_grad, axis=-1, keepdims=True)
        score_grad = (probs * (prob_grad - delta) * scale).astype(jnp.bfloat16)
        kg_ref[:, cols] = lax.dot_general(
            score_grad, q, (((0,), (0,)), ((), ())), preferred_element_type=jnp.float32
        ).astype(kg_ref.dtype)


def attend(key_rows, value_rows, query, cotangent, factor, visible, first_head, heads):
    samples = visible.shape[0]
    seq = query.shape[1] // samples
    keys = key_rows.shape[0] // samples
    fac = jnp.full((8, 128), factor, jnp.float32)
    group = heads if first_head % heads == 0 else 1
    wide = group * HD
    text_spec = pl.BlockSpec(
        (None, seq, wide), lambda s, h, vis: (0, s, first_head // group + h)
    )
    image_spec = pl.BlockSpec((keys, wide), lambda s, h, vis: (s, h))
    return pl.pallas_call(
        attend_kernel,
        grid_spec=pltpu.PrefetchScalarGridSpec(
            num_scalar_prefetch=1,
            grid=(samples, heads // group),
            in_specs=[
                pl.BlockSpec((8, 128), lambda s, h, vis: (0, 0)),
                text_spec,
                image_spec,
                image_spec,
                text_spec,
            ],
            out_specs=[
                pl.BlockSpec((seq, wide), lambda s, h, vis: (s, h)),
                image_spec,
                image_spec,
            ],
        ),
        out_shape=[
            jax.ShapeDtypeStruct((query.shape[1], heads * HD), jnp.bfloat16),
            jax.ShapeDtypeStruct(key_rows.shape, jnp.bfloat16),
            jax.ShapeDtypeStruct(key_rows.shape, jnp.bfloat16),
        ],
    )(visible, fac, query, key_rows, value_rows, cotangent)


def back_product(grad_rows, weight):
    return lax.dot_general(
        grad_rows, weight, (((1,), (1,)), ((), ())), preferred_element_type=jnp.float32
    )


def exchange(value, axis, swap):
    return lax.ppermute(value.astype(jnp.bfloat16), axis, swap).astype(jnp.float32)


def chip_reduce(term, layer, swap):
    core = lax.axis_index("core")
    quarter = term.shape[0] // 4
    rows = term.reshape(4, quarter, term.shape[1])
    even = rows[0::2]
    odd = rows[1::2]
    keep = jnp.where(core == 0, even, odd)
    give = jnp.where(core == 0, odd, even)
    halves = keep + exchange(give, "core", swap)
    split = (halves.shape[2] // HD * 5 // 8) * HD
    first = halves[:, :, :split]
    second = halves[:, :, split:]
    mine = jnp.where(layer == 0, first[0], first[1])
    other = jnp.where(layer == 0, first[1], first[0])
    summed = mine + exchange(other, "layer", swap)
    rounded = summed.astype(jnp.bfloat16).astype(jnp.float32)
    total_first = rounded + exchange(summed, "tx", swap)
    rounded = second.astype(jnp.bfloat16).astype(jnp.float32)
    across = rounded + exchange(second, "tx", swap)
    mine = jnp.where(layer == 0, across[0], across[1])
    other = jnp.where(layer == 0, across[1], across[0])
    total_second = mine + exchange(other, "layer", swap)
    total = jnp.concatenate([total_first, total_second], axis=1).astype(jnp.bfloat16)
    partner = lax.ppermute(total, "core", swap)
    return jnp.where(
        core == 0,
        jnp.concatenate([total, partner], axis=0),
        jnp.concatenate([partner, total], axis=0),
    )


def shards(vision_tokens, key_weight, value_weight, queries, gate, visible, out_grad):
    layer = lax.axis_index("layer")
    micro = lax.axis_index("micro")
    width = key_weight.shape[1]
    heads = width // HD
    if heads % sum(PARTS) == 0:
        unit = heads // sum(PARTS)
        sizes = [part * unit * HD for part in PARTS]
    else:
        chunks = min(CHUNKS, heads)
        sizes = [width // chunks] * chunks
    chunks = len(sizes)
    starts = [sum(sizes[:j]) for j in range(chunks)]
    gate_value = lax.dynamic_index_in_dim(gate, layer, 0, keepdims=False)
    factor = jnp.tanh(gate_value)
    own_visible = lax.dynamic_index_in_dim(visible, micro, 0, keepdims=False)
    swap = [(0, 1), (1, 0)]
    paired = lax.axis_size("layer") == 2
    if paired:
        partner = lax.ppermute(vision_tokens, "layer", swap)
        all_rows = jnp.where(
            layer == 0,
            jnp.concatenate([vision_tokens, partner], axis=0),
            jnp.concatenate([partner, vision_tokens], axis=0),
        )
    else:
        all_rows = lax.all_gather(vision_tokens, "layer", axis=0, tiled=True)
    term = None
    pieces = []
    gathered = {}

    micros = lax.axis_size("micro")

    def line_gather(own):
        ups, downs = [], []
        up, down = own, own
        for r in range(1, micros):
            up = lax.ppermute(up, "micro", [(i, i + 1) for i in range(r - 1, micros - 1)])
            down = lax.ppermute(down, "micro", [(i + 1, i) for i in range(r - 1, micros - 1)])
            ups.append(up)
            downs.append(down)
        blocks = []
        for q in range(micros):
            which = jnp.where(q == micro, 0, jnp.where(q < micro, micro - q, micros - 1 + q - micro))
            blocks.append(lax.select_n(which, own, *ups, *downs))
        return jnp.concatenate(blocks, axis=1)

    def fetch(j, after):
        cols = slice(starts[j], starts[j] + sizes[j])
        stacked = jnp.stack([key_weight[:, cols], value_weight[:, cols]])
        if after is not None:
            stacked, _ = lax.optimization_barrier((stacked, after))
        if RELAY:
            gathered[j] = line_gather(stacked)
        else:
            gathered[j] = lax.all_gather(stacked, "micro", axis=1, tiled=True)

    for j in range(min(AHEAD, chunks)):
        fetch(j, None)
    for j in range(chunks):
        cols = slice(starts[j], starts[j] + sizes[j])
        stacked = gathered.pop(j)
        if term is not None:
            stacked, _ = lax.optimization_barrier((stacked, term))
        w_key = stacked[0]
        w_value = stacked[1]
        key_rows = jnp.dot(all_rows, w_key, preferred_element_type=jnp.float32).astype(jnp.bfloat16)
        value_rows = jnp.dot(all_rows, w_value, preferred_element_type=jnp.float32).astype(
            jnp.bfloat16
        )
        attended, key_grad, value_grad = attend(
            key_rows,
            value_rows,
            queries,
            out_grad,
            factor,
            own_visible,
            starts[j] // HD,
            sizes[j] // HD,
        )
        pieces.append(attended)
        part = back_product(key_grad, w_key) + back_product(value_grad, w_value)
        term = part if term is None else term + part
        if j + AHEAD < chunks:
            fetch(j + AHEAD, term)
    attended = jnp.concatenate(pieces, axis=1)
    if paired and lax.axis_size("tx") == 2 and lax.axis_size("core") == 2:
        owned = chip_reduce(term, layer, swap)
    else:
        part = lax.psum_scatter(
            term.astype(jnp.bfloat16), "layer", scatter_dimension=0, tiled=True
        )
        owned = lax.psum(part, ("tx", "core"))
    return (attended[None], owned)


def solution(mesh):
    sections, tensors = mesh.devices.shape
    grid = Mesh(
        np.asarray(mesh.devices).reshape(MICRO, sections // MICRO, tensors // 2, 2),
        ("micro", "layer", "tx", "core"),
    )
    rows = ("micro", "layer")
    cols = ("tx", "core")
    placed = (
        P(rows, None),
        P(rows, cols),
        P(rows, cols),
        P(rows, None, cols),
        P(),
        P(),
        P(rows, None, cols),
    )
    return jax.shard_map(
        shards,
        mesh=grid,
        in_specs=placed,
        out_specs=(P(rows, None, cols), P(rows, None)),
        check_vma=False,
    )
```

```python
import jax
import jax.numpy as jnp
import numpy as np
from jax import lax
from jax.experimental import pallas as pl
from jax.experimental.pallas import tpu as pltpu
from jax.sharding import Mesh
from jax.sharding import PartitionSpec as P

HD = 128
IMG_TOK = 64
TBLOCK = 64
IMGS = 2
MICRO = 4
CHUNKS = 4
PARTS = (3, 1)
AHEAD = 8
RELAY = False


def attend_kernel(vis_ref, fac_ref, q_ref, k_ref, v_ref, g_ref, att_ref, kg_ref, vg_ref):
    sample = pl.program_id(0)
    seq = q_ref.shape[0]
    keys = k_ref.shape[0]
    scale = 1.0 / HD**0.5
    factor = fac_ref[0:1, 0:1]
    rows = lax.broadcasted_iota(jnp.int32, (seq, keys), 0) // TBLOCK
    image = lax.broadcasted_iota(jnp.int32, (seq, keys), 1) // IMG_TOK
    sees = jnp.full((seq, keys), -1, jnp.int32)
    for b in range(seq // TBLOCK):
        sees = jnp.where(rows == b, vis_ref[sample, b], sees)
    allowed = image == sees
    valid = sees >= 0
    for h in range(q_ref.shape[1] // HD):
        cols = pl.ds(h * HD, HD)
        q = q_ref[:, cols]
        k = k_ref[:, cols]
        v = v_ref[:, cols]
        scores = (
            lax.dot_general(q, k, (((1,), (1,)), ((), ())), preferred_element_type=jnp.float32)
            * scale
        )
        exponent = jnp.where(allowed, jnp.exp(scores), 0.0)
        total = jnp.sum(exponent, axis=-1, keepdims=True)
        probs = jnp.where(valid, exponent / jnp.where(valid, total, 1.0), 0.0)
        probs_b = probs.astype(jnp.bfloat16)
        mixed = jnp.dot(probs_b, v, preferred_element_type=jnp.float32)
        att_ref[:, cols] = (factor * mixed).astype(att_ref.dtype)
        head_grad = (factor * g_ref[:, cols].astype(jnp.float32)).astype(jnp.bfloat16)
        vg_ref[:, cols] = lax.dot_general(
            probs_b, head_grad, (((0,), (0,)), ((), ())), preferred_element_type=jnp.float32
        ).astype(vg_ref.dtype)
        prob_grad = lax.dot_general(
            head_grad, v, (((1,), (1,)), ((), ())), preferred_element_type=jnp.float32
        )
        delta = jnp.sum(probs * prob_grad, axis=-1, keepdims=True)
        score_grad = (probs * (prob_grad - delta) * scale).astype(jnp.bfloat16)
        kg_ref[:, cols] = lax.dot_general(
            score_grad, q, (((0,), (0,)), ((), ())), preferred_element_type=jnp.float32
        ).astype(kg_ref.dtype)


def attend(key_rows, value_rows, query, cotangent, factor, visible, first_head, heads):
    samples = visible.shape[0]
    seq = query.shape[1] // samples
    keys = key_rows.shape[0] // samples
    fac = jnp.full((8, 128), factor, jnp.float32)
    group = heads if first_head % heads == 0 else 1
    wide = group * HD
    text_spec = pl.BlockSpec(
        (None, seq, wide), lambda s, h, vis: (0, s, first_head // group + h)
    )
    image_spec = pl.BlockSpec((keys, wide), lambda s, h, vis: (s, h))
    return pl.pallas_call(
        attend_kernel,
        grid_spec=pltpu.PrefetchScalarGridSpec(
            num_scalar_prefetch=1,
            grid=(samples, heads // group),
            in_specs=[
                pl.BlockSpec((8, 128), lambda s, h, vis: (0, 0)),
                text_spec,
                image_spec,
                image_spec,
                text_spec,
            ],
            out_specs=[
                pl.BlockSpec((seq, wide), lambda s, h, vis: (s, h)),
                image_spec,
                image_spec,
            ],
        ),
        out_shape=[
            jax.ShapeDtypeStruct((query.shape[1], heads * HD), jnp.bfloat16),
            jax.ShapeDtypeStruct(key_rows.shape, jnp.bfloat16),
            jax.ShapeDtypeStruct(key_rows.shape, jnp.bfloat16),
        ],
    )(visible, fac, query, key_rows, value_rows, cotangent)


def back_product(grad_rows, weight):
    return lax.dot_general(
        grad_rows, weight, (((1,), (1,)), ((), ())), preferred_element_type=jnp.float32
    )


def exchange(value, axis, swap):
    return lax.ppermute(value.astype(jnp.bfloat16), axis, swap).astype(jnp.float32)


def chip_reduce(term, layer, swap):
    core = lax.axis_index("core")
    quarter = term.shape[0] // 4
    rows = term.reshape(4, quarter, term.shape[1])
    even = rows[0::2]
    odd = rows[1::2]
    keep = jnp.where(core == 0, even, odd)
    give = jnp.where(core == 0, odd, even)
    halves = keep + exchange(give, "core", swap)
    split = (halves.shape[2] // HD * 5 // 8) * HD
    first = halves[:, :, :split]
    second = halves[:, :, split:]
    mine = jnp.where(layer == 0, first[0], first[1])
    other = jnp.where(layer == 0, first[1], first[0])
    summed = mine + exchange(other, "layer", swap)
    rounded = summed.astype(jnp.bfloat16).astype(jnp.float32)
    total_first = rounded + exchange(summed, "tx", swap)
    rounded = second.astype(jnp.bfloat16).astype(jnp.float32)
    across = rounded + exchange(second, "tx", swap)
    mine = jnp.where(layer == 0, across[0], across[1])
    other = jnp.where(layer == 0, across[1], across[0])
    total_second = mine + exchange(other, "layer", swap)
    total = jnp.concatenate([total_first, total_second], axis=1).astype(jnp.bfloat16)
    partner = lax.ppermute(total, "core", swap)
    return jnp.where(
        core == 0,
        jnp.concatenate([total, partner], axis=0),
        jnp.concatenate([partner, total], axis=0),
    )


def shards(vision_tokens, key_weight, value_weight, queries, gate, visible, out_grad):
    layer = lax.axis_index("layer")
    micro = lax.axis_index("micro")
    width = key_weight.shape[1]
    heads = width // HD
    if heads % sum(PARTS) == 0:
        unit = heads // sum(PARTS)
        sizes = [part * unit * HD for part in PARTS]
    else:
        chunks = min(CHUNKS, heads)
        sizes = [width // chunks] * chunks
    chunks = len(sizes)
    starts = [sum(sizes[:j]) for j in range(chunks)]
    gate_value = lax.dynamic_index_in_dim(gate, layer, 0, keepdims=False)
    factor = jnp.tanh(gate_value)
    own_visible = lax.dynamic_index_in_dim(visible, micro, 0, keepdims=False)
    swap = [(0, 1), (1, 0)]
    paired = lax.axis_size("layer") == 2
    if paired:
        partner = lax.ppermute(vision_tokens, "layer", swap)
        all_rows = jnp.where(
            layer == 0,
            jnp.concatenate([vision_tokens, partner], axis=0),
            jnp.concatenate([partner, vision_tokens], axis=0),
        )
    else:
        all_rows = lax.all_gather(vision_tokens, "layer", axis=0, tiled=True)
    term = None
    pieces = []
    gathered = {}

    micros = lax.axis_size("micro")

    def line_gather(own):
        ups, downs = [], []
        up, down = own, own
        for r in range(1, micros):
            up = lax.ppermute(up, "micro", [(i, i + 1) for i in range(r - 1, micros - 1)])
            down = lax.ppermute(down, "micro", [(i + 1, i) for i in range(r - 1, micros - 1)])
            ups.append(up)
            downs.append(down)
        blocks = []
        for q in range(micros):
            which = jnp.where(q == micro, 0, jnp.where(q < micro, micro - q, micros - 1 + q - micro))
            blocks.append(lax.select_n(which, own, *ups, *downs))
        return jnp.concatenate(blocks, axis=1)

    def fetch(j, after):
        cols = slice(starts[j], starts[j] + sizes[j])
        stacked = jnp.stack([key_weight[:, cols], value_weight[:, cols]])
        if after is not None:
            stacked, _ = lax.optimization_barrier((stacked, after))
        if RELAY:
            gathered[j] = line_gather(stacked)
        else:
            gathered[j] = lax.all_gather(stacked, "micro", axis=1, tiled=True)

    for j in range(min(AHEAD, chunks)):
        fetch(j, None)
    for j in range(chunks):
        cols = slice(starts[j], starts[j] + sizes[j])
        stacked = gathered.pop(j)
        if term is not None:
            stacked, _ = lax.optimization_barrier((stacked, term))
        w_key = stacked[0]
        w_value = stacked[1]
        projected = jnp.einsum(
            "td,sdc->stc", all_rows, stacked, preferred_element_type=jnp.float32
        ).astype(jnp.bfloat16)
        key_rows = projected[0]
        value_rows = projected[1]
        attended, key_grad, value_grad = attend(
            key_rows,
            value_rows,
            queries,
            out_grad,
            factor,
            own_visible,
            starts[j] // HD,
            sizes[j] // HD,
        )
        pieces.append(attended)
        part = back_product(key_grad, w_key) + back_product(value_grad, w_value)
        term = part if term is None else term + part
        if j + AHEAD < chunks:
            fetch(j + AHEAD, term)
    attended = jnp.concatenate(pieces, axis=1)
    if paired and lax.axis_size("tx") == 2 and lax.axis_size("core") == 2:
        owned = chip_reduce(term, layer, swap)
    else:
        part = lax.psum_scatter(
            term.astype(jnp.bfloat16), "layer", scatter_dimension=0, tiled=True
        )
        owned = lax.psum(part, ("tx", "core"))
    return (attended[None], owned)


def solution(mesh):
    sections, tensors = mesh.devices.shape
    grid = Mesh(
        np.asarray(mesh.devices).reshape(MICRO, sections // MICRO, tensors // 2, 2),
        ("micro", "layer", "tx", "core"),
    )
    rows = ("micro", "layer")
    cols = ("tx", "core")
    placed = (
        P(rows, None),
        P(rows, cols),
        P(rows, cols),
        P(rows, None, cols),
        P(),
        P(),
        P(rows, None, cols),
    )
    return jax.shard_map(
        shards,
        mesh=grid,
        in_specs=placed,
        out_specs=(P(rows, None, cols), P(rows, None)),
        check_vma=False,
    )
```

```python
import jax
import jax.numpy as jnp
import numpy as np
from jax import lax
from jax.experimental import pallas as pl
from jax.experimental.pallas import tpu as pltpu
from jax.sharding import Mesh
from jax.sharding import PartitionSpec as P

HD = 128
IMG_TOK = 64
TBLOCK = 64
IMGS = 2
MICRO = 4
CHUNKS = 4
PARTS = (3, 1)
AHEAD = 8
RELAY = False


def attend_kernel(vis_ref, fac_ref, q_ref, k_ref, v_ref, g_ref, *rest):
    att_ref, kg_ref, vg_ref = rest[-3:]
    sample = pl.program_id(0)
    seq = q_ref.shape[0]
    keys = k_ref.shape[0]
    scale = 1.0 / HD**0.5
    factor = fac_ref[0:1, 0:1]
    rows = lax.broadcasted_iota(jnp.int32, (seq, keys), 0) // TBLOCK
    image = lax.broadcasted_iota(jnp.int32, (seq, keys), 1) // IMG_TOK
    sees = jnp.full((seq, keys), -1, jnp.int32)
    for b in range(seq // TBLOCK):
        sees = jnp.where(rows == b, vis_ref[sample, b], sees)
    allowed = image == sees
    valid = sees >= 0
    for h in range(q_ref.shape[1] // HD):
        cols = pl.ds(h * HD, HD)
        q = q_ref[:, cols]
        k = k_ref[:, cols]
        v = v_ref[:, cols]
        scores = (
            lax.dot_general(q, k, (((1,), (1,)), ((), ())), preferred_element_type=jnp.float32)
            * scale
        )
        exponent = jnp.where(allowed, jnp.exp(scores), 0.0)
        total = jnp.sum(exponent, axis=-1, keepdims=True)
        probs = jnp.where(valid, exponent / jnp.where(valid, total, 1.0), 0.0)
        probs_b = probs.astype(jnp.bfloat16)
        mixed = jnp.dot(probs_b, v, preferred_element_type=jnp.float32)
        att_ref[:, cols] = (factor * mixed).astype(att_ref.dtype)
        head_grad = (factor * g_ref[:, cols].astype(jnp.float32)).astype(jnp.bfloat16)
        vg_ref[:, cols] = lax.dot_general(
            probs_b, head_grad, (((0,), (0,)), ((), ())), preferred_element_type=jnp.float32
        ).astype(vg_ref.dtype)
        prob_grad = lax.dot_general(
            head_grad, v, (((1,), (1,)), ((), ())), preferred_element_type=jnp.float32
        )
        delta = jnp.sum(probs * prob_grad, axis=-1, keepdims=True)
        score_grad = (probs * (prob_grad - delta) * scale).astype(jnp.bfloat16)
        kg_ref[:, cols] = lax.dot_general(
            score_grad, q, (((0,), (0,)), ((), ())), preferred_element_type=jnp.float32
        ).astype(kg_ref.dtype)


def attend(key_rows, value_rows, query, cotangent, factor, visible, first_head, heads, previous):
    samples = visible.shape[0]
    seq = query.shape[1] // samples
    keys = key_rows.shape[0] // samples
    fac = jnp.full((8, 128), factor, jnp.float32)
    group = heads if first_head % heads == 0 else 1
    wide = group * HD
    text_spec = pl.BlockSpec(
        (None, seq, wide), lambda s, h, vis: (0, s, first_head // group + h)
    )
    image_spec = pl.BlockSpec((keys, wide), lambda s, h, vis: (s, h))
    return pl.pallas_call(
        attend_kernel,
        grid_spec=pltpu.PrefetchScalarGridSpec(
            num_scalar_prefetch=1,
            grid=(samples, heads // group),
            in_specs=[
                pl.BlockSpec((8, 128), lambda s, h, vis: (0, 0)),
                text_spec,
                image_spec,
                image_spec,
                text_spec,
            ]
            + [pl.BlockSpec(memory_space=pl.ANY)] * len(previous),
            out_specs=[
                pl.BlockSpec((seq, wide), lambda s, h, vis: (s, first_head // group + h)),
                image_spec,
                image_spec,
            ],
        ),
        out_shape=[
            jax.ShapeDtypeStruct(query.shape[1:], jnp.bfloat16),
            jax.ShapeDtypeStruct(key_rows.shape, jnp.bfloat16),
            jax.ShapeDtypeStruct(key_rows.shape, jnp.bfloat16),
        ],
        input_output_aliases={6: 0} if previous else {},
    )(visible, fac, query, key_rows, value_rows, cotangent, *previous)


def back_product(grad_rows, weight):
    return lax.dot_general(
        grad_rows, weight, (((1,), (1,)), ((), ())), preferred_element_type=jnp.float32
    )


def exchange(value, axis, swap):
    return lax.ppermute(value.astype(jnp.bfloat16), axis, swap).astype(jnp.float32)


def chip_reduce(term, layer, swap):
    core = lax.axis_index("core")
    quarter = term.shape[0] // 4
    rows = term.reshape(4, quarter, term.shape[1])
    even = rows[0::2]
    odd = rows[1::2]
    keep = jnp.where(core == 0, even, odd)
    give = jnp.where(core == 0, odd, even)
    halves = keep + exchange(give, "core", swap)
    split = (halves.shape[2] // HD * 5 // 8) * HD
    first = halves[:, :, :split]
    second = halves[:, :, split:]
    mine = jnp.where(layer == 0, first[0], first[1])
    other = jnp.where(layer == 0, first[1], first[0])
    summed = mine + exchange(other, "layer", swap)
    rounded = summed.astype(jnp.bfloat16).astype(jnp.float32)
    total_first = rounded + exchange(summed, "tx", swap)
    rounded = second.astype(jnp.bfloat16).astype(jnp.float32)
    across = rounded + exchange(second, "tx", swap)
    mine = jnp.where(layer == 0, across[0], across[1])
    other = jnp.where(layer == 0, across[1], across[0])
    total_second = mine + exchange(other, "layer", swap)
    total = jnp.concatenate([total_first, total_second], axis=1).astype(jnp.bfloat16)
    partner = lax.ppermute(total, "core", swap)
    return jnp.where(
        core == 0,
        jnp.concatenate([total, partner], axis=0),
        jnp.concatenate([partner, total], axis=0),
    )


def shards(vision_tokens, key_weight, value_weight, queries, gate, visible, out_grad):
    layer = lax.axis_index("layer")
    micro = lax.axis_index("micro")
    width = key_weight.shape[1]
    heads = width // HD
    if heads % sum(PARTS) == 0:
        unit = heads // sum(PARTS)
        sizes = [part * unit * HD for part in PARTS]
    else:
        chunks = min(CHUNKS, heads)
        sizes = [width // chunks] * chunks
    chunks = len(sizes)
    starts = [sum(sizes[:j]) for j in range(chunks)]
    gate_value = lax.dynamic_index_in_dim(gate, layer, 0, keepdims=False)
    factor = jnp.tanh(gate_value)
    own_visible = lax.dynamic_index_in_dim(visible, micro, 0, keepdims=False)
    swap = [(0, 1), (1, 0)]
    paired = lax.axis_size("layer") == 2
    if paired:
        partner = lax.ppermute(vision_tokens, "layer", swap)
        all_rows = jnp.where(
            layer == 0,
            jnp.concatenate([vision_tokens, partner], axis=0),
            jnp.concatenate([partner, vision_tokens], axis=0),
        )
    else:
        all_rows = lax.all_gather(vision_tokens, "layer", axis=0, tiled=True)
    term = None
    pieces = []
    gathered = {}

    micros = lax.axis_size("micro")

    def line_gather(own):
        ups, downs = [], []
        up, down = own, own
        for r in range(1, micros):
            up = lax.ppermute(up, "micro", [(i, i + 1) for i in range(r - 1, micros - 1)])
            down = lax.ppermute(down, "micro", [(i + 1, i) for i in range(r - 1, micros - 1)])
            ups.append(up)
            downs.append(down)
        blocks = []
        for q in range(micros):
            which = jnp.where(q == micro, 0, jnp.where(q < micro, micro - q, micros - 1 + q - micro))
            blocks.append(lax.select_n(which, own, *ups, *downs))
        return jnp.concatenate(blocks, axis=1)

    def fetch(j, after):
        cols = slice(starts[j], starts[j] + sizes[j])
        stacked = jnp.stack([key_weight[:, cols], value_weight[:, cols]])
        if after is not None:
            stacked, _ = lax.optimization_barrier((stacked, after))
        if RELAY:
            gathered[j] = line_gather(stacked)
        else:
            gathered[j] = lax.all_gather(stacked, "micro", axis=1, tiled=True)

    for j in range(min(AHEAD, chunks)):
        fetch(j, None)
    for j in range(chunks):
        cols = slice(starts[j], starts[j] + sizes[j])
        stacked = gathered.pop(j)
        if term is not None:
            stacked, _ = lax.optimization_barrier((stacked, term))
        w_key = stacked[0]
        w_value = stacked[1]
        projected = jnp.einsum(
            "td,sdc->stc", all_rows, stacked, preferred_element_type=jnp.float32
        ).astype(jnp.bfloat16)
        key_rows = projected[0]
        value_rows = projected[1]
        attended, key_grad, value_grad = attend(
            key_rows,
            value_rows,
            queries,
            out_grad,
            factor,
            own_visible,
            starts[j] // HD,
            sizes[j] // HD,
            pieces[-1:],
        )
        pieces = [attended]
        part = back_product(key_grad, w_key) + back_product(value_grad, w_value)
        term = part if term is None else term + part
        if j + AHEAD < chunks:
            fetch(j + AHEAD, term)
    attended = pieces[0]
    if paired and lax.axis_size("tx") == 2 and lax.axis_size("core") == 2:
        owned = chip_reduce(term, layer, swap)
    else:
        part = lax.psum_scatter(
            term.astype(jnp.bfloat16), "layer", scatter_dimension=0, tiled=True
        )
        owned = lax.psum(part, ("tx", "core"))
    return (attended[None], owned)


def solution(mesh):
    sections, tensors = mesh.devices.shape
    grid = Mesh(
        np.asarray(mesh.devices).reshape(MICRO, sections // MICRO, tensors // 2, 2),
        ("micro", "layer", "tx", "core"),
    )
    rows = ("micro", "layer")
    cols = ("tx", "core")
    placed = (
        P(rows, None),
        P(rows, cols),
        P(rows, cols),
        P(rows, None, cols),
        P(),
        P(),
        P(rows, None, cols),
    )
    return jax.shard_map(
        shards,
        mesh=grid,
        in_specs=placed,
        out_specs=(P(rows, None, cols), P(rows, None)),
        check_vma=False,
    )
```
